256 devices in a mesh: expert: 32 (over z_hi, y, core), dp: 8 (over z_lo, x).
Axes of the slice: x: 4, y: 4, z: 8 (z_hi: 4, z_lo: 2; z = z_hi * 2 + z_lo), core: 2. Of those that a mesh axis runs over, the one named last changes fastest.
Arguments:
- tokens: bfloat16 [2048, 196, 384], P(('expert', 'dp')), may hold values from -6 to 6
- router: bfloat16 [384, 64], replicated, may hold values from -1 to 65
- expert_in: bfloat16 [64, 384, 1536], P('expert'), may hold values from -2.5 to 2.5
- expert_out: bfloat16 [64, 1536, 384], P('expert'), may hold values from -0.15625 to 0.15625
- out_grad: bfloat16 [2048, 196, 384], P(('expert', 'dp')), may hold values from -6 to 6
Outputs:
- grad_tokens: bfloat16 [2048, 196, 384], P(('expert', 'dp'))
- grad_in: float32 [64, 384, 1536], P('expert', None, 'dp')
- grad_out: float32 [64, 1536, 384], P('expert', 'dp')
- grad_router: float32 [384, 64], replicated
The draws below stay inside these ranges and needn't reach their ends.
All inputs are finite; a program needn't handle non-finite values.
Results may differ from the reference program's by a relative error of at most 0.017.
Values may be sent and summed in bfloat16 or wider, within the bound.
No kernel may reach another device: no remote copies, remote signals or barrier semaphores. Data moves between devices by JAX's collectives and lax.ppermute only.
A program may use at most 64 MiB of HBM per device.

```python
import jax
import jax.numpy as jnp
from jax import lax

D = 384
FF = 1536
PATCHES = 196
IMG_DEV = 8
EXPERTS = 64
IMAGES = 2048


def draw_tokens(key, part):
    keys = jax.random.split(key, 1)
    values = jnp.clip(jax.random.normal(keys[0], (IMAGES, PATCHES, D), jnp.float32), -6.0, 6.0)
    return values.astype(jnp.bfloat16)


def draw_router(key, part):
    values = jnp.clip(jax.random.normal(key, (D, EXPERTS), jnp.float32), -6.0, 6.0) / math_root(D)
    return values.astype(jnp.bfloat16)


def math_root(count):
    return float(count) ** 0.5


def block_levels(rng, extent, cuts, least, largest):
    def one(axis_at, shards_of):
        steps = jax.random.uniform(jax.random.fold_in(jax.random.fold_in(rng, 6), axis_at), (shards_of,), jnp.float32, least / len(cuts), largest / len(cuts))
        return jnp.repeat(jnp.exp(steps), extent[axis_at] // shards_of).reshape((-1,) + (1,) * (len(extent) - axis_at - 1))

    factor_of = one(*cuts[0])
    for cut in cuts[1:]:
        factor_of = factor_of * one(*cut)
    return factor_of


def gaussian(rng, shape, spread, most, shards=(), dtype=jnp.bfloat16):
    array = spread * jax.random.normal(rng, shape, jnp.float32)
    if shards:
        array = array * block_levels(rng, shape, shards, -0.22, 0.18)
    return jnp.clip(array, -most, most).astype(dtype)


def setup_inputs(seed: int = 0) -> dict:
    splits = jax.random.split(jax.random.key(seed), 6)
    tokens = draw_tokens(jax.random.fold_in(splits[5], 71), 0)
    router = draw_router(jax.random.fold_in(splits[5], 71), 0)
    expert_in = gaussian(splits[2], (EXPERTS, D, FF), (D // 64) ** -0.5, 2.5, ((0, 32),))
    expert_out = gaussian(splits[3], (EXPERTS, FF, D), FF ** -0.5, 0.15625, ((0, 32),))
    out_grad = gaussian(splits[4], (IMAGES, PATCHES, D), 1.0, 6.0, ((0, 256),))
    return {"tokens": tokens, "router": router, "expert_in": expert_in, "expert_out": expert_out, "out_grad": out_grad}


def reference(tokens, router, expert_in, expert_out, out_grad):
    router_wide = router.astype(jnp.float32)

    def slot_side(block):
        images, cotangent = block
        logits = jnp.einsum('bpd,ds->bps', images.astype(jnp.float32), router_wide)
        dispatch_low = jax.nn.softmax(logits, axis=1).astype(jnp.bfloat16)
        combine_low = jax.nn.softmax(logits, axis=2).astype(jnp.bfloat16)
        slots = jnp.einsum('bps,bpd->bsd', dispatch_low.astype(jnp.float32), images.astype(jnp.float32)).astype(jnp.bfloat16)
        slot_grads = jnp.einsum('bps,bpd->bsd', combine_low.astype(jnp.float32), cotangent.astype(jnp.float32)).astype(jnp.bfloat16)
        return (slots, slot_grads)
    shaped_tokens = tokens.reshape((-1, IMG_DEV, PATCHES, D))
    shaped_grads = out_grad.reshape((-1, IMG_DEV, PATCHES, D))
    slots, slot_grads = lax.map(slot_side, (shaped_tokens, shaped_grads))
    slots = slots.reshape((IMAGES, EXPERTS, D))
    slot_grads = slot_grads.reshape((IMAGES, EXPERTS, D))

    def expert_side(block):
        inputs, grads, first, second = block
        hidden = jnp.dot(inputs, first, preferred_element_type=jnp.float32)
        activated, gelu_back = jax.vjp(jax.nn.gelu, hidden)
        activated_low = activated.astype(jnp.bfloat16)
        slot_out = jnp.dot(activated_low, second, preferred_element_type=jnp.float32).astype(jnp.bfloat16)
        act_grad = jnp.dot(grads, second.T, preferred_element_type=jnp.float32)
        hidden_grad = gelu_back(act_grad)[0].astype(jnp.bfloat16)
        slot_in_grad = jnp.dot(hidden_grad, first.T, preferred_element_type=jnp.float32).astype(jnp.bfloat16)
        first_grad = jnp.dot(inputs.T, hidden_grad, preferred_element_type=jnp.float32)
        second_grad = jnp.dot(activated_low.T, grads, preferred_element_type=jnp.float32)
        return (slot_out, slot_in_grad, first_grad, second_grad)
    slot_out, slot_in_grad, grad_in, grad_out = lax.map(expert_side, (jnp.moveaxis(slots, 1, 0), jnp.moveaxis(slot_grads, 1, 0), expert_in, expert_out))
    slot_out = jnp.moveaxis(slot_out, 0, 1).reshape((-1, IMG_DEV, EXPERTS, D))
    slot_in_grad = jnp.moveaxis(slot_in_grad, 0, 1).reshape((-1, IMG_DEV, EXPERTS, D))

    def token_side(block):
        images, cotangent, outputs, inputs_grad = block
        images_wide = images.astype(jnp.float32)
        logits = jnp.einsum('bpd,ds->bps', images_wide, router_wide)
        dispatch = jax.nn.softmax(logits, axis=1)
        combine = jax.nn.softmax(logits, axis=2)
        dispatch_low = dispatch.astype(jnp.bfloat16)
        combine_grad = jnp.einsum('bpd,bsd->bps', cotangent.astype(jnp.float32), outputs.astype(jnp.float32))
        dispatch_grad = jnp.einsum('bpd,bsd->bps', images_wide, inputs_grad.astype(jnp.float32))
        logit_grad = dispatch * (dispatch_grad - lax.optimization_barrier(jnp.sum(dispatch * dispatch_grad, axis=1, keepdims=True)))
        logit_grad = logit_grad + combine * (combine_grad - lax.optimization_barrier(jnp.sum(combine * combine_grad, axis=2, keepdims=True)))
        logit_low = logit_grad.astype(jnp.bfloat16).astype(jnp.float32)
        first_part = jnp.einsum('bps,bsd->bpd', dispatch_low.astype(jnp.float32), inputs_grad.astype(jnp.float32))
        second_part = jnp.einsum('bps,ds->bpd', logit_low, router_wide)
        token_grad = (first_part + second_part).astype(jnp.bfloat16)
        router_term = jnp.einsum('bpd,bps->ds', images_wide, logit_low)
        return (token_grad, router_term)
    grad_tokens, router_terms = lax.map(token_side, (shaped_tokens, shaped_grads, slot_out, slot_in_grad))
    grad_tokens = grad_tokens.reshape((IMAGES, PATCHES, D))
    grad_router = lax.optimization_barrier(jnp.sum(router_terms, axis=0))
    return (grad_tokens, grad_in, grad_out, grad_router)
```

```python
import jax
import jax.numpy as jnp
from jax import lax
from jax.sharding import PartitionSpec as P


def _sum_everywhere(term, axes):
    count = 1
    for name in axes:
        count *= lax.axis_size(name)
    pieces = term.reshape(count, term.size // count)
    mine = jnp.sum(lax.all_to_all(pieces, axes, 0, 0, tiled=True), axis=0, keepdims=True)
    spread = jnp.broadcast_to(mine, pieces.shape)
    return lax.all_to_all(spread, axes, 0, 0, tiled=True).reshape(term.shape)


def on_device(tokens, router, expert_in, expert_out, out_grad):
    logits = jnp.einsum("bpd,ds->bps", tokens, router, preferred_element_type=jnp.float32)
    dispatch = jax.nn.softmax(logits, axis=1)
    combine = jax.nn.softmax(logits, axis=2)
    dispatch_low = dispatch.astype(jnp.bfloat16)
    combine_low = combine.astype(jnp.bfloat16)
    slots = jnp.einsum(
        "bps,bpd->bsd", dispatch_low, tokens, preferred_element_type=jnp.float32
    ).astype(jnp.bfloat16)
    slot_grads = jnp.einsum(
        "bps,bpd->bsd", combine_low, out_grad, preferred_element_type=jnp.float32
    ).astype(jnp.bfloat16)
    slots_here, grads_here = (
        lax.all_to_all(slots, "expert", split_axis=1, concat_axis=0, tiled=True),
        lax.all_to_all(slot_grads, "expert", split_axis=1, concat_axis=0, tiled=True),
    )
    hidden = jnp.einsum("rjd,jdf->rjf", slots_here, expert_in, preferred_element_type=jnp.float32)
    activated, gelu_back = jax.vjp(jax.nn.gelu, hidden)
    activated_low = activated.astype(jnp.bfloat16)
    outputs_here = jnp.einsum(
        "rjf,jfd->rjd", activated_low, expert_out, preferred_element_type=jnp.float32
    ).astype(jnp.bfloat16)
    act_grad = jnp.einsum(
        "rjd,jfd->rjf", grads_here, expert_out, preferred_element_type=jnp.float32
    )
    hidden_grad = gelu_back(act_grad)[0].astype(jnp.bfloat16)
    input_grad_here = jnp.einsum(
        "rjf,jdf->rjd", hidden_grad, expert_in, preferred_element_type=jnp.float32
    ).astype(jnp.bfloat16)
    outputs, inputs_grad = (
        lax.all_to_all(outputs_here, "expert", split_axis=0, concat_axis=1, tiled=True),
        lax.all_to_all(input_grad_here, "expert", split_axis=0, concat_axis=1, tiled=True),
    )
    first_term = jnp.einsum(
        "rjd,rjf->jdf", slots_here, hidden_grad, preferred_element_type=jnp.float32
    )
    second_term = jnp.einsum(
        "rjf,rjd->jfd", activated_low, grads_here, preferred_element_type=jnp.float32
    )
    grad_in = lax.psum_scatter(
        first_term.astype(jnp.bfloat16), "dp", scatter_dimension=2, tiled=True
    ).astype(jnp.float32)
    grad_out = lax.psum_scatter(
        second_term.astype(jnp.bfloat16), "dp", scatter_dimension=1, tiled=True
    ).astype(jnp.float32)
    combine_grad = jnp.einsum("bpd,bsd->bps", out_grad, outputs, preferred_element_type=jnp.float32)
    dispatch_grad = jnp.einsum(
        "bpd,bsd->bps", tokens, inputs_grad, preferred_element_type=jnp.float32
    )
    logit_grad = dispatch * (
        dispatch_grad - jnp.sum(dispatch * dispatch_grad, axis=1, keepdims=True)
    )
    logit_grad = logit_grad + combine * (
        combine_grad - jnp.sum(combine * combine_grad, axis=2, keepdims=True)
    )
    logit_low = logit_grad.astype(jnp.bfloat16)
    first_part = jnp.einsum(
        "bps,bsd->bpd", dispatch_low, inputs_grad, preferred_element_type=jnp.float32
    )
    second_part = jnp.einsum("bps,ds->bpd", logit_low, router, preferred_element_type=jnp.float32)
    grad_tokens = (first_part + second_part).astype(jnp.bfloat16)
    router_term = jnp.einsum("bpd,bps->ds", tokens, logit_low, preferred_element_type=jnp.float32)
    grad_router = _sum_everywhere(router_term, ("expert", "dp"))
    return (grad_tokens, grad_in, grad_out, grad_router)


def solution(mesh):
    placed = (
        P(("expert", "dp"), None, None),
        P(),
        P("expert", None, None),
        P("expert", None, None),
        P(("expert", "dp"), None, None),
    )
    return jax.shard_map(
        on_device,
        mesh=mesh,
        in_specs=placed,
        out_specs=(
            P(("expert", "dp"), None, None),
            P("expert", None, "dp"),
            P("expert", "dp", None),
            P(),
        ),
        check_vma=False,
    )
```

```python
import jax
import jax.numpy as jnp
from jax import lax
from jax.sharding import PartitionSpec as P


def _sum_everywhere(term, axes):
    count = 1
    for name in axes:
        count *= lax.axis_size(name)
    pieces = term.reshape(count, term.size // count)
    mine = jnp.sum(lax.all_to_all(pieces, axes, 0, 0, tiled=True), axis=0, keepdims=True)
    spread = jnp.broadcast_to(mine, pieces.shape)
    return lax.all_to_all(spread, axes, 0, 0, tiled=True).reshape(term.shape)


def _reduced(value):
    return lax.optimization_barrier(value)


def _softmax(logits, axis):
    top = _reduced(jnp.max(logits, axis=axis, keepdims=True))
    raised = jnp.exp(logits - top)
    return raised / _reduced(jnp.sum(raised, axis=axis, keepdims=True))


def on_device(tokens, router, expert_in, expert_out, out_grad):
    logits = jnp.einsum("bpd,ds->bps", tokens, router, preferred_element_type=jnp.float32)
    dispatch = _softmax(logits, 1)
    combine = _softmax(logits, 2)
    dispatch_low = dispatch.astype(jnp.bfloat16)
    combine_low = combine.astype(jnp.bfloat16)
    slots = jnp.einsum(
        "bps,bpd->bsd", dispatch_low, tokens, preferred_element_type=jnp.float32
    ).astype(jnp.bfloat16)
    slot_grads = jnp.einsum(
        "bps,bpd->bsd", combine_low, out_grad, preferred_element_type=jnp.float32
    ).astype(jnp.bfloat16)
    slots_here, grads_here = (
        lax.all_to_all(slots, "expert", split_axis=1, concat_axis=0, tiled=True),
        lax.all_to_all(slot_grads, "expert", split_axis=1, concat_axis=0, tiled=True),
    )
    hidden = jnp.einsum("rjd,jdf->rjf", slots_here, expert_in, preferred_element_type=jnp.float32)
    activated, gelu_back = jax.vjp(jax.nn.gelu, hidden)
    activated_low = activated.astype(jnp.bfloat16)
    outputs_here = jnp.einsum(
        "rjf,jfd->rjd", activated_low, expert_out, preferred_element_type=jnp.float32
    ).astype(jnp.bfloat16)
    act_grad = jnp.einsum(
        "rjd,jfd->rjf", grads_here, expert_out, preferred_element_type=jnp.float32
    )
    hidden_grad = gelu_back(act_grad)[0].astype(jnp.bfloat16)
    input_grad_here = jnp.einsum(
        "rjf,jdf->rjd", hidden_grad, expert_in, preferred_element_type=jnp.float32
    ).astype(jnp.bfloat16)
    outputs, inputs_grad = (
        lax.all_to_all(outputs_here, "expert", split_axis=0, concat_axis=1, tiled=True),
        lax.all_to_all(input_grad_here, "expert", split_axis=0, concat_axis=1, tiled=True),
    )
    first_term = jnp.einsum(
        "rjd,rjf->jdf", slots_here, hidden_grad, preferred_element_type=jnp.float32
    )
    second_term = jnp.einsum(
        "rjf,rjd->jfd", activated_low, grads_here, preferred_element_type=jnp.float32
    )
    grad_in = lax.psum_scatter(
        first_term.astype(jnp.bfloat16), "dp", scatter_dimension=2, tiled=True
    ).astype(jnp.float32)
    grad_out = lax.psum_scatter(
        second_term.astype(jnp.bfloat16), "dp", scatter_dimension=1, tiled=True
    ).astype(jnp.float32)
    combine_grad = jnp.einsum("bpd,bsd->bps", out_grad, outputs, preferred_element_type=jnp.float32)
    dispatch_grad = jnp.einsum(
        "bpd,bsd->bps", tokens, inputs_grad, preferred_element_type=jnp.float32
    )
    logit_grad = dispatch * (
        dispatch_grad - _reduced(jnp.sum(dispatch * dispatch_grad, axis=1, keepdims=True))
    )
    logit_grad = logit_grad + combine * (
        combine_grad - _reduced(jnp.sum(combine * combine_grad, axis=2, keepdims=True))
    )
    logit_low = logit_grad.astype(jnp.bfloat16)
    first_part = jnp.einsum(
        "bps,bsd->bpd", dispatch_low, inputs_grad, preferred_element_type=jnp.float32
    )
    second_part = jnp.einsum("bps,ds->bpd", logit_low, router, preferred_element_type=jnp.float32)
    grad_tokens = (first_part + second_part).astype(jnp.bfloat16)
    router_term = jnp.einsum("bpd,bps->ds", tokens, logit_low, preferred_element_type=jnp.float32)
    grad_router = _sum_everywhere(router_term, ("expert", "dp"))
    return (grad_tokens, grad_in, grad_out, grad_router)


def solution(mesh):
    placed = (
        P(("expert", "dp"), None, None),
        P(),
        P("expert", None, None),
        P("expert", None, None),
        P(("expert", "dp"), None, None),
    )
    return jax.shard_map(
        on_device,
        mesh=mesh,
        in_specs=placed,
        out_specs=(
            P(("expert", "dp"), None, None),
            P("expert", None, "dp"),
            P("expert", "dp", None),
            P(),
        ),
        check_vma=False,
    )
```

```python
import jax
import jax.numpy as jnp
from jax import lax
from jax.sharding import PartitionSpec as P


def _sum_everywhere(term, axes):
    count = 1
    for name in axes:
        count *= lax.axis_size(name)
    pieces = term.reshape(count, term.size // count)
    mine = jnp.sum(lax.all_to_all(pieces, axes, 0, 0, tiled=True), axis=0, keepdims=True)
    spread = jnp.broadcast_to(mine, pieces.shape)
    return lax.all_to_all(spread, axes, 0, 0, tiled=True).reshape(term.shape)


def _reduced(value):
    return lax.optimization_barrier(value)


def _softmax(logits, axis):
    top = _reduced(jnp.max(logits, axis=axis, keepdims=True))
    raised = jnp.exp(logits - top)
    return raised / _reduced(jnp.sum(raised, axis=axis, keepdims=True))


def on_device(tokens, router, expert_in, expert_out, out_grad):
    logits = jnp.einsum("bpd,ds->bps", tokens, router, preferred_element_type=jnp.float32)
    dispatch = _softmax(logits, 1)
    combine = _softmax(logits, 2)
    dispatch_low = dispatch.astype(jnp.bfloat16)
    combine_low = combine.astype(jnp.bfloat16)
    slots = jnp.einsum(
        "bps,bpd->bsd", dispatch_low, tokens, preferred_element_type=jnp.float32
    ).astype(jnp.bfloat16)
    slot_grads = jnp.einsum(
        "bps,bpd->bsd", combine_low, out_grad, preferred_element_type=jnp.float32
    ).astype(jnp.bfloat16)
    sent = lax.all_to_all(
        jnp.stack([slots, slot_grads]), "expert", split_axis=2, concat_axis=1, tiled=True
    )
    slots_here, grads_here = sent[0], sent[1]
    hidden = jnp.einsum("rjd,jdf->rjf", slots_here, expert_in, preferred_element_type=jnp.float32)
    activated, gelu_back = jax.vjp(jax.nn.gelu, hidden)
    activated_low = activated.astype(jnp.bfloat16)
    outputs_here = jnp.einsum(
        "rjf,jfd->rjd", activated_low, expert_out, preferred_element_type=jnp.float32
    ).astype(jnp.bfloat16)
    act_grad = jnp.einsum(
        "rjd,jfd->rjf", grads_here, expert_out, preferred_element_type=jnp.float32
    )
    hidden_grad = gelu_back(act_grad)[0].astype(jnp.bfloat16)
    input_grad_here = jnp.einsum(
        "rjf,jdf->rjd", hidden_grad, expert_in, preferred_element_type=jnp.float32
    ).astype(jnp.bfloat16)
    returned = lax.all_to_all(
        jnp.stack([outputs_here, input_grad_here]), "expert", split_axis=1, concat_axis=2, tiled=True
    )
    outputs, inputs_grad = returned[0], returned[1]
    first_term = jnp.einsum(
        "rjd,rjf->jdf", slots_here, hidden_grad, preferred_element_type=jnp.float32
    )
    second_term = jnp.einsum(
        "rjf,rjd->jfd", activated_low, grads_here, preferred_element_type=jnp.float32
    )
    grad_in = lax.psum_scatter(
        first_term.astype(jnp.bfloat16), "dp", scatter_dimension=2, tiled=True
    ).astype(jnp.float32)
    grad_out = lax.psum_scatter(
        second_term.astype(jnp.bfloat16), "dp", scatter_dimension=1, tiled=True
    ).astype(jnp.float32)
    combine_grad = jnp.einsum("bpd,bsd->bps", out_grad, outputs, preferred_element_type=jnp.float32)
    dispatch_grad = jnp.einsum(
        "bpd,bsd->bps", tokens, inputs_grad, preferred_element_type=jnp.float32
    )
    logit_grad = dispatch * (
        dispatch_grad - _reduced(jnp.sum(dispatch * dispatch_grad, axis=1, keepdims=True))
    )
    logit_grad = logit_grad + combine * (
        combine_grad - _reduced(jnp.sum(combine * combine_grad, axis=2, keepdims=True))
    )
    logit_low = logit_grad.astype(jnp.bfloat16)
    first_part = jnp.einsum(
        "bps,bsd->bpd", dispatch_low, inputs_grad, preferred_element_type=jnp.float32
    )
    second_part = jnp.einsum("bps,ds->bpd", logit_low, router, preferred_element_type=jnp.float32)
    grad_tokens = (first_part + second_part).astype(jnp.bfloat16)
    router_term = jnp.einsum("bpd,bps->ds", tokens, logit_low, preferred_element_type=jnp.float32)
    grad_router = _sum_everywhere(router_term, ("expert", "dp"))
    return (grad_tokens, grad_in, grad_out, grad_router)


def solution(mesh):
    placed = (
        P(("expert", "dp"), None, None),
        P(),
        P("expert", None, None),
        P("expert", None, None),
        P(("expert", "dp"), None, None),
    )
    return jax.shard_map(
        on_device,
        mesh=mesh,
        in_specs=placed,
        out_specs=(
            P(("expert", "dp"), None, None),
            P("expert", None, "dp"),
            P("expert", "dp", None),
            P(),
        ),
        check_vma=False,
    )
```

```python
import jax
import jax.numpy as jnp
from jax import lax
from jax.sharding import PartitionSpec as P


def _sum_everywhere(term, axes):
    count = 1
    for name in axes:
        count *= lax.axis_size(name)
    pieces = term.reshape(count, term.size // count)
    mine = jnp.sum(lax.all_to_all(pieces, axes, 0, 0, tiled=True), axis=0, keepdims=True)
    spread = jnp.broadcast_to(mine, pieces.shape)
    return lax.all_to_all(spread, axes, 0, 0, tiled=True).reshape(term.shape)


def _reduced(value):
    return lax.optimization_barrier(value)


def _softmax(logits, axis):
    top = _reduced(jnp.max(logits, axis=axis, keepdims=True))
    raised = jnp.exp(logits - top)
    return raised / _reduced(jnp.sum(raised, axis=axis, keepdims=True))


def _token_forward(tokens, router, out_grad):
    logits = jnp.einsum("bpd,ds->bps", tokens, router, preferred_element_type=jnp.float32)
    dispatch = _softmax(logits, 1)
    combine = _softmax(logits, 2)
    dispatch_low = dispatch.astype(jnp.bfloat16)
    combine_low = combine.astype(jnp.bfloat16)
    slots = jnp.einsum(
        "bps,bpd->bsd", dispatch_low, tokens, preferred_element_type=jnp.float32
    ).astype(jnp.bfloat16)
    slot_grads = jnp.einsum(
        "bps,bpd->bsd", combine_low, out_grad, preferred_element_type=jnp.float32
    ).astype(jnp.bfloat16)
    sent = lax.all_to_all(
        jnp.stack([slots, slot_grads]), "expert", split_axis=2, concat_axis=1, tiled=True
    )
    return (dispatch, combine, dispatch_low), sent


def _expert_side(sent, expert_in, expert_out):
    slots_here, grads_here = sent[0], sent[1]
    hidden = jnp.einsum("rjd,jdf->rjf", slots_here, expert_in, preferred_element_type=jnp.float32)
    activated, gelu_back = jax.vjp(jax.nn.gelu, hidden)
    activated_low = activated.astype(jnp.bfloat16)
    outputs_here = jnp.einsum(
        "rjf,jfd->rjd", activated_low, expert_out, preferred_element_type=jnp.float32
    ).astype(jnp.bfloat16)
    act_grad = jnp.einsum(
        "rjd,jfd->rjf", grads_here, expert_out, preferred_element_type=jnp.float32
    )
    hidden_grad = gelu_back(act_grad)[0].astype(jnp.bfloat16)
    input_grad_here = jnp.einsum(
        "rjf,jdf->rjd", hidden_grad, expert_in, preferred_element_type=jnp.float32
    ).astype(jnp.bfloat16)
    returned = lax.all_to_all(
        jnp.stack([outputs_here, input_grad_here]), "expert", split_axis=1, concat_axis=2, tiled=True
    )
    first_term = jnp.einsum(
        "rjd,rjf->jdf", slots_here, hidden_grad, preferred_element_type=jnp.float32
    )
    second_term = jnp.einsum(
        "rjf,rjd->jfd", activated_low, grads_here, preferred_element_type=jnp.float32
    )
    return returned, first_term, second_term


def _token_backward(tokens, router, out_grad, kept, returned):
    dispatch, combine, dispatch_low = kept
    outputs, inputs_grad = returned[0], returned[1]
    combine_grad = jnp.einsum("bpd,bsd->bps", out_grad, outputs, preferred_element_type=jnp.float32)
    dispatch_grad = jnp.einsum(
        "bpd,bsd->bps", tokens, inputs_grad, preferred_element_type=jnp.float32
    )
    logit_grad = dispatch * (
        dispatch_grad - _reduced(jnp.sum(dispatch * dispatch_grad, axis=1, keepdims=True))
    )
    logit_grad = logit_grad + combine * (
        combine_grad - _reduced(jnp.sum(combine * combine_grad, axis=2, keepdims=True))
    )
    logit_low = logit_grad.astype(jnp.bfloat16)
    first_part = jnp.einsum(
        "bps,bsd->bpd", dispatch_low, inputs_grad, preferred_element_type=jnp.float32
    )
    second_part = jnp.einsum("bps,ds->bpd", logit_low, router, preferred_element_type=jnp.float32)
    grad_tokens = (first_part + second_part).astype(jnp.bfloat16)
    router_term = jnp.einsum("bpd,bps->ds", tokens, logit_low, preferred_element_type=jnp.float32)
    return grad_tokens, router_term


CHUNKS = 2


def on_device(tokens, router, expert_in, expert_out, out_grad):
    size = tokens.shape[0] // CHUNKS
    pieces = [slice(c * size, (c + 1) * size) for c in range(CHUNKS)]
    forward = [_token_forward(tokens[c], router, out_grad[c]) for c in pieces]
    experts = [_expert_side(sent, expert_in, expert_out) for _, sent in forward]
    backward = [
        _token_backward(tokens[c], router, out_grad[c], kept, returned)
        for c, (kept, _), (returned, _, _) in zip(pieces, forward, experts)
    ]
    first_term = sum(e[1] for e in experts)
    second_term = sum(e[2] for e in experts)
    grad_in = lax.psum_scatter(
        first_term.astype(jnp.bfloat16), "dp", scatter_dimension=2, tiled=True
    ).astype(jnp.float32)
    grad_out = lax.psum_scatter(
        second_term.astype(jnp.bfloat16), "dp", scatter_dimension=1, tiled=True
    ).astype(jnp.float32)
    grad_tokens = jnp.concatenate([b[0] for b in backward], axis=0)
    router_term = sum(b[1] for b in backward)
    grad_router = _sum_everywhere(router_term, ("expert", "dp"))
    return (grad_tokens, grad_in, grad_out, grad_router)


def solution(mesh):
    placed = (
        P(("expert", "dp"), None, None),
        P(),
        P("expert", None, None),
        P("expert", None, None),
        P(("expert", "dp"), None, None),
    )
    return jax.shard_map(
        on_device,
        mesh=mesh,
        in_specs=placed,
        out_specs=(
            P(("expert", "dp"), None, None),
            P("expert", None, "dp"),
            P("expert", "dp", None),
            P(),
        ),
        check_vma=False,
    )
```

```python
import jax
import jax.numpy as jnp
from jax import lax
from jax.sharding import PartitionSpec as P


def _sum_everywhere(term, axes):
    count = 1
    for name in axes:
        count *= lax.axis_size(name)
    pieces = term.reshape(count, term.size // count)
    mine = jnp.sum(lax.all_to_all(pieces, axes, 0, 0, tiled=True), axis=0, keepdims=True)
    spread = jnp.broadcast_to(mine, pieces.shape)
    return lax.all_to_all(spread, axes, 0, 0, tiled=True).reshape(term.shape)


def _reduced(value):
    return lax.optimization_barrier(value)


def _softmax(logits, axis):
    top = _reduced(jnp.max(logits, axis=axis, keepdims=True))
    raised = jnp.exp(logits - top)
    return raised / _reduced(jnp.sum(raised, axis=axis, keepdims=True))


def on_device(tokens, router, expert_in, expert_out, out_grad):
    logits = jnp.einsum("bpd,ds->bps", tokens, router, preferred_element_type=jnp.float32)
    dispatch = _softmax(logits, 1)
    combine = _softmax(logits, 2)
    dispatch_low = dispatch.astype(jnp.bfloat16)
    combine_low = combine.astype(jnp.bfloat16)
    slots = jnp.einsum(
        "bps,bpd->bsd", dispatch_low, tokens, preferred_element_type=jnp.float32
    ).astype(jnp.bfloat16)
    slot_grads = jnp.einsum(
        "bps,bpd->bsd", combine_low, out_grad, preferred_element_type=jnp.float32
    ).astype(jnp.bfloat16)
    width = slots.shape[-1]
    sent = lax.all_to_all(
        jnp.concatenate([slots, slot_grads], axis=-1), "expert", split_axis=1, concat_axis=0, tiled=True
    )
    slots_here, grads_here = sent[..., :width], sent[..., width:]
    hidden = jnp.einsum("rjd,jdf->rjf", slots_here, expert_in, preferred_element_type=jnp.float32)
    activated, gelu_back = jax.vjp(jax.nn.gelu, hidden)
    activated_low = activated.astype(jnp.bfloat16)
    outputs_here = jnp.einsum(
        "rjf,jfd->rjd", activated_low, expert_out, preferred_element_type=jnp.float32
    ).astype(jnp.bfloat16)
    act_grad = jnp.einsum(
        "rjd,jfd->rjf", grads_here, expert_out, preferred_element_type=jnp.float32
    )
    hidden_grad = gelu_back(act_grad)[0].astype(jnp.bfloat16)
    input_grad_here = jnp.einsum(
        "rjf,jdf->rjd", hidden_grad, expert_in, preferred_element_type=jnp.float32
    ).astype(jnp.bfloat16)
    returned = lax.all_to_all(
        jnp.concatenate([outputs_here, input_grad_here], axis=-1),
        "expert", split_axis=0, concat_axis=1, tiled=True,
    )
    outputs, inputs_grad = returned[..., :width], returned[..., width:]
    first_term = jnp.einsum(
        "rjd,rjf->jdf", slots_here, hidden_grad, preferred_element_type=jnp.float32
    )
    second_term = jnp.einsum(
        "rjf,rjd->jfd", activated_low, grads_here, preferred_element_type=jnp.float32
    )
    grad_in = lax.psum_scatter(
        first_term.astype(jnp.bfloat16), "dp", scatter_dimension=2, tiled=True
    ).astype(jnp.float32)
    grad_out = lax.psum_scatter(
        second_term.astype(jnp.bfloat16), "dp", scatter_dimension=1, tiled=True
    ).astype(jnp.float32)
    combine_grad = jnp.einsum("bpd,bsd->bps", out_grad, outputs, preferred_element_type=jnp.float32)
    dispatch_grad = jnp.einsum(
        "bpd,bsd->bps", tokens, inputs_grad, preferred_element_type=jnp.float32
    )
    logit_grad = dispatch * (
        dispatch_grad - _reduced(jnp.sum(dispatch * dispatch_grad, axis=1, keepdims=True))
    )
    logit_grad = logit_grad + combine * (
        combine_grad - _reduced(jnp.sum(combine * combine_grad, axis=2, keepdims=True))
    )
    logit_low = logit_grad.astype(jnp.bfloat16)
    first_part = jnp.einsum(
        "bps,bsd->bpd", dispatch_low, inputs_grad, preferred_element_type=jnp.float32
    )
    second_part = jnp.einsum("bps,ds->bpd", logit_low, router, preferred_element_type=jnp.float32)
    grad_tokens = (first_part + second_part).astype(jnp.bfloat16)
    router_term = jnp.einsum("bpd,bps->ds", tokens, logit_low, preferred_element_type=jnp.float32)
    grad_router = _sum_everywhere(router_term, ("expert", "dp"))
    return (grad_tokens, grad_in, grad_out, grad_router)


def solution(mesh):
    placed = (
        P(("expert", "dp"), None, None),
        P(),
        P("expert", None, None),
        P("expert", None, None),
        P(("expert", "dp"), None, None),
    )
    return jax.shard_map(
        on_device,
        mesh=mesh,
        in_specs=placed,
        out_specs=(
            P(("expert", "dp"), None, None),
            P("expert", None, "dp"),
            P("expert", "dp", None),
            P(),
        ),
        check_vma=False,
    )
```

```python
import jax
import jax.numpy as jnp
from jax import lax
from jax.sharding import PartitionSpec as P


def _sum_everywhere(term, axes):
    count = 1
    for name in axes:
        count *= lax.axis_size(name)
    bits = count.bit_length() - 1
    assert 1 << bits == count
    low = 0
    while low < bits:
        width = min(2, bits - low)
        got = [term] + [
            lax.ppermute(term, axes, [(i, i ^ (m << low)) for i in range(count)])
            for m in range(1, 1 << width)
        ]
        while len(got) > 1:
            got = [got[2 * j] + got[2 * j + 1] for j in range(len(got) // 2)]
        term = got[0]
        low += width
    return term


def _reduced(value):
    return lax.optimization_barrier(value)


def _softmax(logits, axis):
    top = _reduced(jnp.max(logits, axis=axis, keepdims=True))
    raised = jnp.exp(logits - top)
    return raised / _reduced(jnp.sum(raised, axis=axis, keepdims=True))


def on_device(tokens, router, expert_in, expert_out, out_grad):
    logits = jnp.einsum("bpd,ds->bps", tokens, router, preferred_element_type=jnp.float32)
    dispatch = _softmax(logits, 1)
    combine = _softmax(logits, 2)
    dispatch_low = dispatch.astype(jnp.bfloat16)
    combine_low = combine.astype(jnp.bfloat16)
    slots = jnp.einsum(
        "bps,bpd->bsd", dispatch_low, tokens, preferred_element_type=jnp.float32
    ).astype(jnp.bfloat16)
    slot_grads = jnp.einsum(
        "bps,bpd->bsd", combine_low, out_grad, preferred_element_type=jnp.float32
    ).astype(jnp.bfloat16)
    sent = lax.all_to_all(
        jnp.stack([slots, slot_grads]), "expert", split_axis=2, concat_axis=1, tiled=True
    )
    slots_here, grads_here = sent[0], sent[1]
    hidden = jnp.einsum("rjd,jdf->rjf", slots_here, expert_in, preferred_element_type=jnp.float32)
    activated, gelu_back = jax.vjp(jax.nn.gelu, hidden)
    activated_low = activated.astype(jnp.bfloat16)
    outputs_here = jnp.einsum(
        "rjf,jfd->rjd", activated_low, expert_out, preferred_element_type=jnp.float32
    ).astype(jnp.bfloat16)
    act_grad = jnp.einsum(
        "rjd,jfd->rjf", grads_here, expert_out, preferred_element_type=jnp.float32
    )
    hidden_grad = gelu_back(act_grad)[0].astype(jnp.bfloat16)
    input_grad_here = jnp.einsum(
        "rjf,jdf->rjd", hidden_grad, expert_in, preferred_element_type=jnp.float32
    ).astype(jnp.bfloat16)
    returned = lax.all_to_all(
        jnp.stack([outputs_here, input_grad_here]), "expert", split_axis=1, concat_axis=2, tiled=True
    )
    outputs, inputs_grad = returned[0], returned[1]
    first_term = jnp.einsum(
        "rjd,rjf->jdf", slots_here, hidden_grad, preferred_element_type=jnp.float32
    )
    second_term = jnp.einsum(
        "rjf,rjd->jfd", activated_low, grads_here, preferred_element_type=jnp.float32
    )
    grad_in = lax.psum_scatter(
        first_term.astype(jnp.bfloat16), "dp", scatter_dimension=2, tiled=True
    ).astype(jnp.float32)
    grad_out = lax.psum_scatter(
        second_term.astype(jnp.bfloat16), "dp", scatter_dimension=1, tiled=True
    ).astype(jnp.float32)
    combine_grad = jnp.einsum("bpd,bsd->bps", out_grad, outputs, preferred_element_type=jnp.float32)
    dispatch_grad = jnp.einsum(
        "bpd,bsd->bps", tokens, inputs_grad, preferred_element_type=jnp.float32
    )
    logit_grad = dispatch * (
        dispatch_grad - _reduced(jnp.sum(dispatch * dispatch_grad, axis=1, keepdims=True))
    )
    logit_grad = logit_grad + combine * (
        combine_grad - _reduced(jnp.sum(combine * combine_grad, axis=2, keepdims=True))
    )
    logit_low = logit_grad.astype(jnp.bfloat16)
    first_part = jnp.einsum(
        "bps,bsd->bpd", dispatch_low, inputs_grad, preferred_element_type=jnp.float32
    )
    second_part = jnp.einsum("bps,ds->bpd", logit_low, router, preferred_element_type=jnp.float32)
    grad_tokens = (first_part + second_part).astype(jnp.bfloat16)
    router_term = jnp.einsum("bpd,bps->ds", tokens, logit_low, preferred_element_type=jnp.float32)
    grad_router = _sum_everywhere(router_term, ("expert", "dp"))
    return (grad_tokens, grad_in, grad_out, grad_router)


def solution(mesh):
    placed = (
        P(("expert", "dp"), None, None),
        P(),
        P("expert", None, None),
        P("expert", None, None),
        P(("expert", "dp"), None, None),
    )
    return jax.shard_map(
        on_device,
        mesh=mesh,
        in_specs=placed,
        out_specs=(
            P(("expert", "dp"), None, None),
            P("expert", None, "dp"),
            P("expert", "dp", None),
            P(),
        ),
        check_vma=False,
    )
```

```python
import jax
import jax.numpy as jnp
from jax import lax
from jax.sharding import PartitionSpec as P


def _sum_everywhere(term, axes):
    count = 1
    for name in axes:
        count *= lax.axis_size(name)
    bits = count.bit_length() - 1
    assert 1 << bits == count
    low = 0
    while low < bits:
        width = min(2, bits - low)
        got = [term] + [
            lax.ppermute(term, axes, [(i, i ^ (m << low)) for i in range(count)])
            for m in range(1, 1 << width)
        ]
        while len(got) > 1:
            got = [got[2 * j] + got[2 * j + 1] for j in range(len(got) // 2)]
        term = got[0]
        low += width
    return term


def _reduced(value):
    return lax.optimization_barrier(value)


def _softmax(logits, axis):
    top = _reduced(jnp.max(logits, axis=axis, keepdims=True))
    raised = jnp.exp(logits - top)
    return raised / _reduced(jnp.sum(raised, axis=axis, keepdims=True))


def on_device(tokens, router, expert_in, expert_out, out_grad):
    logits = jnp.einsum("bpd,ds->bsp", tokens, router, preferred_element_type=jnp.float32)
    dispatch = _softmax(logits, 2)
    combine = _softmax(logits, 1)
    dispatch_low = dispatch.astype(jnp.bfloat16)
    combine_low = combine.astype(jnp.bfloat16)
    slots = jnp.einsum(
        "bsp,bpd->bsd", dispatch_low, tokens, preferred_element_type=jnp.float32
    ).astype(jnp.bfloat16)
    slot_grads = jnp.einsum(
        "bsp,bpd->bsd", combine_low, out_grad, preferred_element_type=jnp.float32
    ).astype(jnp.bfloat16)
    sent = lax.all_to_all(
        jnp.stack([slots, slot_grads]), "expert", split_axis=2, concat_axis=1, tiled=True
    )
    slots_here, grads_here = sent[0], sent[1]
    hidden = jnp.einsum("rjd,jdf->rjf", slots_here, expert_in, preferred_element_type=jnp.float32)
    activated, gelu_back = jax.vjp(jax.nn.gelu, hidden)
    activated_low = activated.astype(jnp.bfloat16)
    outputs_here = jnp.einsum(
        "rjf,jfd->rjd", activated_low, expert_out, preferred_element_type=jnp.float32
    ).astype(jnp.bfloat16)
    act_grad = jnp.einsum(
        "rjd,jfd->rjf", grads_here, expert_out, preferred_element_type=jnp.float32
    )
    hidden_grad = gelu_back(act_grad)[0].astype(jnp.bfloat16)
    input_grad_here = jnp.einsum(
        "rjf,jdf->rjd", hidden_grad, expert_in, preferred_element_type=jnp.float32
    ).astype(jnp.bfloat16)
    returned = lax.all_to_all(
        jnp.stack([outputs_here, input_grad_here]), "expert", split_axis=1, concat_axis=2, tiled=True
    )
    outputs, inputs_grad = returned[0], returned[1]
    first_term = jnp.einsum(
        "rjd,rjf->jdf", slots_here, hidden_grad, preferred_element_type=jnp.float32
    )
    second_term = jnp.einsum(
        "rjf,rjd->jfd", activated_low, grads_here, preferred_element_type=jnp.float32
    )
    grad_in = lax.psum_scatter(
        first_term.astype(jnp.bfloat16), "dp", scatter_dimension=2, tiled=True
    ).astype(jnp.float32)
    grad_out = lax.psum_scatter(
        second_term.astype(jnp.bfloat16), "dp", scatter_dimension=1, tiled=True
    ).astype(jnp.float32)
    combine_grad = jnp.einsum("bpd,bsd->bsp", out_grad, outputs, preferred_element_type=jnp.float32)
    dispatch_grad = jnp.einsum(
        "bpd,bsd->bsp", tokens, inputs_grad, preferred_element_type=jnp.float32
    )
    logit_grad = dispatch * (
        dispatch_grad - _reduced(jnp.sum(dispatch * dispatch_grad, axis=2, keepdims=True))
    )
    logit_grad = logit_grad + combine * (
        combine_grad - _reduced(jnp.sum(combine * combine_grad, axis=1, keepdims=True))
    )
    logit_low = logit_grad.astype(jnp.bfloat16)
    first_part = jnp.einsum(
        "bsp,bsd->bpd", dispatch_low, inputs_grad, preferred_element_type=jnp.float32
    )
    second_part = jnp.einsum("bsp,ds->bpd", logit_low, router, preferred_element_type=jnp.float32)
    grad_tokens = (first_part + second_part).astype(jnp.bfloat16)
    router_term = jnp.einsum("bpd,bsp->ds", tokens, logit_low, preferred_element_type=jnp.float32)
    grad_router = _sum_everywhere(router_term, ("expert", "dp"))
    return (grad_tokens, grad_in, grad_out, grad_router)


def solution(mesh):
    placed = (
        P(("expert", "dp"), None, None),
        P(),
        P("expert", None, None),
        P("expert", None, None),
        P(("expert", "dp"), None, None),
    )
    return jax.shard_map(
        on_device,
        mesh=mesh,
        in_specs=placed,
        out_specs=(
            P(("expert", "dp"), None, None),
            P("expert", None, "dp"),
            P("expert", "dp", None),
            P(),
        ),
        check_vma=False,
    )
```

```python
import jax
import jax.numpy as jnp
from jax import lax
from jax.sharding import PartitionSpec as P


def _sum_everywhere(term, axes):
    count = 1
    for name in axes:
        count *= lax.axis_size(name)
    bits = count.bit_length() - 1
    assert 1 << bits == count
    low = 0
    while low < bits:
        width = min(2, bits - low)
        got = [term] + [
            lax.ppermute(term, axes, [(i, i ^ (m << low)) for i in range(count)])
            for m in range(1, 1 << width)
        ]
        while len(got) > 1:
            got = [got[2 * j] + got[2 * j + 1] for j in range(len(got) // 2)]
        term = got[0]
        low += width
    return term


def _reduced(value):
    return lax.optimization_barrier(value)


def _softmax(logits, axis):
    top = _reduced(jnp.max(logits, axis=axis, keepdims=True))
    raised = jnp.exp(logits - top)
    return raised / _reduced(jnp.sum(raised, axis=axis, keepdims=True))


def on_device(tokens, router, expert_in, expert_out, out_grad):
    logits = jnp.einsum("bpd,ds->bsp", tokens, router, preferred_element_type=jnp.float32)
    dispatch = _softmax(logits, 2)
    combine = _softmax(logits, 1)
    dispatch_low = dispatch.astype(jnp.bfloat16)
    combine_low = combine.astype(jnp.bfloat16)
    slots = jnp.einsum(
        "bsp,bpd->bsd", dispatch_low, tokens, preferred_element_type=jnp.float32
    ).astype(jnp.bfloat16)
    slot_grads = jnp.einsum(
        "bsp,bpd->bsd", combine_low, out_grad, preferred_element_type=jnp.float32
    ).astype(jnp.bfloat16)
    sent = lax.all_to_all(
        jnp.stack([slots, slot_grads]), "expert", split_axis=2, concat_axis=1, tiled=True
    )
    slots_here, grads_here = sent[0], sent[1]
    hidden = jnp.einsum("rjd,jdf->rjf", slots_here, expert_in, preferred_element_type=jnp.float32)
    activated_low = jax.nn.gelu(hidden).astype(jnp.bfloat16)
    outputs_here = jnp.einsum(
        "rjf,jfd->rjd", activated_low, expert_out, preferred_element_type=jnp.float32
    ).astype(jnp.bfloat16)
    act_grad = jnp.einsum(
        "rjd,jfd->rjf", grads_here, expert_out, preferred_element_type=jnp.float32
    )
    slots_again, act_grad = lax.optimization_barrier((slots_here, act_grad))
    hidden = jnp.einsum("rjd,jdf->rjf", slots_again, expert_in, preferred_element_type=jnp.float32)
    hidden_grad = jax.vjp(jax.nn.gelu, hidden)[1](act_grad)[0].astype(jnp.bfloat16)
    input_grad_here = jnp.einsum(
        "rjf,jdf->rjd", hidden_grad, expert_in, preferred_element_type=jnp.float32
    ).astype(jnp.bfloat16)
    returned = lax.all_to_all(
        jnp.stack([outputs_here, input_grad_here]), "expert", split_axis=1, concat_axis=2, tiled=True
    )
    outputs, inputs_grad = returned[0], returned[1]
    first_term = jnp.einsum(
        "rjd,rjf->jdf", slots_here, hidden_grad, preferred_element_type=jnp.float32
    )
    second_term = jnp.einsum(
        "rjf,rjd->jfd", activated_low, grads_here, preferred_element_type=jnp.float32
    )
    grad_in = lax.psum_scatter(
        first_term.astype(jnp.bfloat16), "dp", scatter_dimension=2, tiled=True
    ).astype(jnp.float32)
    grad_out = lax.psum_scatter(
        second_term.astype(jnp.bfloat16), "dp", scatter_dimension=1, tiled=True
    ).astype(jnp.float32)
    combine_grad = jnp.einsum("bpd,bsd->bsp", out_grad, outputs, preferred_element_type=jnp.float32)
    dispatch_grad = jnp.einsum(
        "bpd,bsd->bsp", tokens, inputs_grad, preferred_element_type=jnp.float32
    )
    logit_grad = dispatch * (
        dispatch_grad - _reduced(jnp.sum(dispatch * dispatch_grad, axis=2, keepdims=True))
    )
    logit_grad = logit_grad + combine * (
        combine_grad - _reduced(jnp.sum(combine * combine_grad, axis=1, keepdims=True))
    )
    logit_low = logit_grad.astype(jnp.bfloat16)
    first_part = jnp.einsum(
        "bsp,bsd->bpd", dispatch_low, inputs_grad, preferred_element_type=jnp.float32
    )
    second_part = jnp.einsum("bsp,ds->bpd", logit_low, router, preferred_element_type=jnp.float32)
    grad_tokens = (first_part + second_part).astype(jnp.bfloat16)
    router_term = jnp.einsum("bpd,bsp->ds", tokens, logit_low, preferred_element_type=jnp.float32)
    grad_router = _sum_everywhere(router_term, ("expert", "dp"))
    return (grad_tokens, grad_in, grad_out, grad_router)


def solution(mesh):
    placed = (
        P(("expert", "dp"), None, None),
        P(),
        P("expert", None, None),
        P("expert", None, None),
        P(("expert", "dp"), None, None),
    )
    return jax.shard_map(
        on_device,
        mesh=mesh,
        in_specs=placed,
        out_specs=(
            P(("expert", "dp"), None, None),
            P("expert", None, "dp"),
            P("expert", "dp", None),
            P(),
        ),
        check_vma=False,
    )
```

```python
import jax
import jax.numpy as jnp
from jax import lax
from jax.sharding import PartitionSpec as P


def _sum_everywhere(term, axes):
    count = 1
    for name in axes:
        count *= lax.axis_size(name)
    pieces = term.reshape(count, term.size // count)
    mine = jnp.sum(lax.all_to_all(pieces, axes, 0, 0, tiled=True), axis=0, keepdims=True)
    spread = jnp.broadcast_to(mine, pieces.shape)
    return lax.all_to_all(spread, axes, 0, 0, tiled=True).reshape(term.shape)


def _reduced(value):
    return lax.optimization_barrier(value)


def _softmax(logits, axis):
    top = _reduced(jnp.max(logits, axis=axis, keepdims=True))
    raised = jnp.exp(logits - top)
    return raised / _reduced(jnp.sum(raised, axis=axis, keepdims=True))


def on_device(tokens, router, expert_in, expert_out, out_grad):
    logits = jnp.einsum("bpd,ds->bsp", tokens, router, preferred_element_type=jnp.float32)
    dispatch = _softmax(logits, 2)
    combine = _softmax(logits, 1)
    dispatch_low = dispatch.astype(jnp.bfloat16)
    combine_low = combine.astype(jnp.bfloat16)
    slots = jnp.einsum(
        "bsp,bpd->bsd", dispatch_low, tokens, preferred_element_type=jnp.float32
    ).astype(jnp.bfloat16)
    slot_grads = jnp.einsum(
        "bsp,bpd->bsd", combine_low, out_grad, preferred_element_type=jnp.float32
    ).astype(jnp.bfloat16)
    sent = lax.all_to_all(
        jnp.stack([slots, slot_grads]), "expert", split_axis=2, concat_axis=1, tiled=True
    )
    slots_here, grads_here = sent[0], sent[1]
    hidden = jnp.einsum("rjd,jdf->rjf", slots_here, expert_in, preferred_element_type=jnp.float32)
    activated_low = jax.nn.gelu(hidden).astype(jnp.bfloat16)
    outputs_here = jnp.einsum(
        "rjf,jfd->rjd", activated_low, expert_out, preferred_element_type=jnp.float32
    ).astype(jnp.bfloat16)
    act_grad = jnp.einsum(
        "rjd,jfd->rjf", grads_here, expert_out, preferred_element_type=jnp.float32
    )
    slots_again, act_grad = lax.optimization_barrier((slots_here, act_grad))
    hidden = jnp.einsum("rjd,jdf->rjf", slots_again, expert_in, preferred_element_type=jnp.float32)
    hidden_grad = jax.vjp(jax.nn.gelu, hidden)[1](act_grad)[0].astype(jnp.bfloat16)
    input_grad_here = jnp.einsum(
        "rjf,jdf->rjd", hidden_grad, expert_in, preferred_element_type=jnp.float32
    ).astype(jnp.bfloat16)
    returned = lax.all_to_all(
        jnp.stack([outputs_here, input_grad_here]), "expert", split_axis=1, concat_axis=2, tiled=True
    )
    outputs, inputs_grad = returned[0], returned[1]
    first_term = jnp.einsum(
        "rjd,rjf->jdf", slots_here, hidden_grad, preferred_element_type=jnp.float32
    )
    second_term = jnp.einsum(
        "rjf,rjd->jfd", activated_low, grads_here, preferred_element_type=jnp.float32
    )
    grad_in = lax.psum_scatter(
        first_term.astype(jnp.bfloat16), "dp", scatter_dimension=2, tiled=True
    ).astype(jnp.float32)
    grad_out = lax.psum_scatter(
        second_term.astype(jnp.bfloat16), "dp", scatter_dimension=1, tiled=True
    ).astype(jnp.float32)
    combine_grad = jnp.einsum("bpd,bsd->bsp", out_grad, outputs, preferred_element_type=jnp.float32)
    dispatch_grad = jnp.einsum(
        "bpd,bsd->bsp", tokens, inputs_grad, preferred_element_type=jnp.float32
    )
    logit_grad = dispatch * (
        dispatch_grad - _reduced(jnp.sum(dispatch * dispatch_grad, axis=2, keepdims=True))
    )
    logit_grad = logit_grad + combine * (
        combine_grad - _reduced(jnp.sum(combine * combine_grad, axis=1, keepdims=True))
    )
    logit_low = logit_grad.astype(jnp.bfloat16)
    first_part = jnp.einsum(
        "bsp,bsd->bpd", dispatch_low, inputs_grad, preferred_element_type=jnp.float32
    )
    second_part = jnp.einsum("bsp,ds->bpd", logit_low, router, preferred_element_type=jnp.float32)
    grad_tokens = (first_part + second_part).astype(jnp.bfloat16)
    router_term = jnp.einsum("bpd,bsp->ds", tokens, logit_low, preferred_element_type=jnp.float32)
    grad_router = _sum_everywhere(router_term, ("expert", "dp"))
    return (grad_tokens, grad_in, grad_out, grad_router)


def solution(mesh):
    placed = (
        P(("expert", "dp"), None, None),
        P(),
        P("expert", None, None),
        P("expert", None, None),
        P(("expert", "dp"), None, None),
    )
    return jax.shard_map(
        on_device,
        mesh=mesh,
        in_specs=placed,
        out_specs=(
            P(("expert", "dp"), None, None),
            P("expert", None, "dp"),
            P("expert", "dp", None),
            P(),
        ),
        check_vma=False,
    )
```

```python
import jax
import jax.numpy as jnp
from jax import lax
from jax.sharding import PartitionSpec as P


def _tree(got):
    while len(got) > 1:
        got = [got[2 * j] + got[2 * j + 1] for j in range(len(got) // 2)]
    return got[0]


def _sum_everywhere(term, axes):
    count = 1
    for name in axes:
        count *= lax.axis_size(name)
    bits = count.bit_length() - 1
    assert 1 << bits == count and bits % 2 == 0
    pairs = lambda m: [(i, i ^ m) for i in range(count)]
    low = lax.axis_index(axes) % 4
    pieces = term.reshape(4, term.size // 4)
    got = [lax.dynamic_index_in_dim(pieces, low, 0, keepdims=False)]
    for m in range(1, 4):
        part = lax.dynamic_index_in_dim(pieces, low ^ m, 0, keepdims=False)
        got.append(lax.ppermute(part, axes, pairs(m)))
    mine = _tree(got)
    for shift in range(2, bits, 2):
        mine = _tree([mine] + [lax.ppermute(mine, axes, pairs(m << shift)) for m in range(1, 4)])
    got = [mine] + [lax.ppermute(mine, axes, pairs(m)) for m in range(1, 4)]
    return jnp.stack([lax.select_n(low ^ q, *got) for q in range(4)]).reshape(term.shape)


def _reduced(value):
    return lax.optimization_barrier(value)


def _softmax(logits, axis):
    top = _reduced(jnp.max(logits, axis=axis, keepdims=True))
    raised = jnp.exp(logits - top)
    return raised / _reduced(jnp.sum(raised, axis=axis, keepdims=True))


def on_device(tokens, router, expert_in, expert_out, out_grad):
    logits = jnp.einsum("bpd,ds->bsp", tokens, router, preferred_element_type=jnp.float32)
    dispatch = _softmax(logits, 2)
    combine = _softmax(logits, 1)
    dispatch_low = dispatch.astype(jnp.bfloat16)
    combine_low = combine.astype(jnp.bfloat16)
    slots = jnp.einsum(
        "bsp,bpd->bsd", dispatch_low, tokens, preferred_element_type=jnp.float32
    ).astype(jnp.bfloat16)
    slot_grads = jnp.einsum(
        "bsp,bpd->bsd", combine_low, out_grad, preferred_element_type=jnp.float32
    ).astype(jnp.bfloat16)
    sent = lax.all_to_all(
        jnp.stack([slots, slot_grads]), "expert", split_axis=2, concat_axis=1, tiled=True
    )
    slots_here, grads_here = sent[0], sent[1]
    hidden = jnp.einsum("rjd,jdf->rjf", slots_here, expert_in, preferred_element_type=jnp.float32)
    activated_low = jax.nn.gelu(hidden).astype(jnp.bfloat16)
    outputs_here = jnp.einsum(
        "rjf,jfd->rjd", activated_low, expert_out, preferred_element_type=jnp.float32
    ).astype(jnp.bfloat16)
    act_grad = jnp.einsum(
        "rjd,jfd->rjf", grads_here, expert_out, preferred_element_type=jnp.float32
    )
    slots_again, act_grad = lax.optimization_barrier((slots_here, act_grad))
    hidden = jnp.einsum("rjd,jdf->rjf", slots_again, expert_in, preferred_element_type=jnp.float32)
    hidden_grad = jax.vjp(jax.nn.gelu, hidden)[1](act_grad)[0].astype(jnp.bfloat16)
    input_grad_here = jnp.einsum(
        "rjf,jdf->rjd", hidden_grad, expert_in, preferred_element_type=jnp.float32
    ).astype(jnp.bfloat16)
    returned = lax.all_to_all(
        jnp.stack([outputs_here, input_grad_here]), "expert", split_axis=1, concat_axis=2, tiled=True
    )
    outputs, inputs_grad = returned[0], returned[1]
    first_term = jnp.einsum(
        "rjd,rjf->jdf", slots_here, hidden_grad, preferred_element_type=jnp.float32
    )
    second_term = jnp.einsum(
        "rjf,rjd->jfd", activated_low, grads_here, preferred_element_type=jnp.float32
    )
    grad_in = lax.psum_scatter(
        first_term.astype(jnp.bfloat16), "dp", scatter_dimension=2, tiled=True
    ).astype(jnp.float32)
    grad_out = lax.psum_scatter(
        second_term.astype(jnp.bfloat16), "dp", scatter_dimension=1, tiled=True
    ).astype(jnp.float32)
    combine_grad = jnp.einsum("bpd,bsd->bsp", out_grad, outputs, preferred_element_type=jnp.float32)
    dispatch_grad = jnp.einsum(
        "bpd,bsd->bsp", tokens, inputs_grad, preferred_element_type=jnp.float32
    )
    logit_grad = dispatch * (
        dispatch_grad - _reduced(jnp.sum(dispatch * dispatch_grad, axis=2, keepdims=True))
    )
    logit_grad = logit_grad + combine * (
        combine_grad - _reduced(jnp.sum(combine * combine_grad, axis=1, keepdims=True))
    )
    logit_low = logit_grad.astype(jnp.bfloat16)
    first_part = jnp.einsum(
        "bsp,bsd->bpd", dispatch_low, inputs_grad, preferred_element_type=jnp.float32
    )
    second_part = jnp.einsum("bsp,ds->bpd", logit_low, router, preferred_element_type=jnp.float32)
    grad_tokens = (first_part + second_part).astype(jnp.bfloat16)
    router_term = jnp.einsum("bpd,bsp->ds", tokens, logit_low, preferred_element_type=jnp.float32)
    grad_router = _sum_everywhere(router_term, ("expert", "dp"))
    return (grad_tokens, grad_in, grad_out, grad_router)


def solution(mesh):
    placed = (
        P(("expert", "dp"), None, None),
        P(),
        P("expert", None, None),
        P("expert", None, None),
        P(("expert", "dp"), None, None),
    )
    return jax.shard_map(
        on_device,
        mesh=mesh,
        in_specs=placed,
        out_specs=(
            P(("expert", "dp"), None, None),
            P("expert", None, "dp"),
            P("expert", "dp", None),
            P(),
        ),
        check_vma=False,
    )
```

```python
import jax
import jax.numpy as jnp
from jax import lax
from jax.sharding import PartitionSpec as P


def _tree(got):
    while len(got) > 1:
        got = [got[2 * j] + got[2 * j + 1] for j in range(len(got) // 2)]
    return got[0]


def _sum_everywhere(term, axes):
    count = 1
    for name in axes:
        count *= lax.axis_size(name)
    bits = count.bit_length() - 1
    assert 1 << bits == count and bits % 2 == 0
    pairs = lambda m: [(i, i ^ m) for i in range(count)]
    low = lax.axis_index(axes) % 4
    pieces = term.reshape(4, term.size // 4)
    got = [lax.dynamic_index_in_dim(pieces, low, 0, keepdims=False)]
    for m in range(1, 4):
        part = lax.dynamic_index_in_dim(pieces, low ^ m, 0, keepdims=False)
        got.append(lax.ppermute(part, axes, pairs(m)))
    mine = _tree(got)
    for shift in range(2, bits, 2):
        mine = _tree([mine] + [lax.ppermute(mine, axes, pairs(m << shift)) for m in range(1, 4)])
    got = [mine] + [lax.ppermute(mine, axes, pairs(m)) for m in range(1, 4)]
    return jnp.stack([lax.select_n(low ^ q, *got) for q in range(4)]).reshape(term.shape)


def _reduced(value):
    return lax.optimization_barrier(value)


def _softmax(logits, axis):
    top = _reduced(jnp.max(logits, axis=axis, keepdims=True))
    raised = jnp.exp(logits - top)
    return raised / _reduced(jnp.sum(raised, axis=axis, keepdims=True))


def on_device(tokens, router, expert_in, expert_out, out_grad):
    logits = jnp.einsum("bpd,ds->bsp", tokens, router, preferred_element_type=jnp.float32)
    dispatch = _softmax(logits, 2)
    combine = _softmax(logits, 1)
    dispatch_low = dispatch.astype(jnp.bfloat16)
    combine_low = combine.astype(jnp.bfloat16)
    slots = jnp.einsum(
        "bsp,bpd->bsd", dispatch_low, tokens, preferred_element_type=jnp.float32
    ).astype(jnp.bfloat16)
    slot_grads = jnp.einsum(
        "bsp,bpd->bsd", combine_low, out_grad, preferred_element_type=jnp.float32
    ).astype(jnp.bfloat16)
    sent = lax.all_to_all(
        jnp.stack([slots, slot_grads]), "expert", split_axis=2, concat_axis=1, tiled=True
    )
    slots_here, grads_here = sent[0], sent[1]
    hidden = jnp.einsum("rjd,jdf->rjf", slots_here, expert_in, preferred_element_type=jnp.float32)
    activated_low = jax.nn.gelu(hidden).astype(jnp.bfloat16)
    outputs_here = jnp.einsum(
        "rjf,jfd->rjd", activated_low, expert_out, preferred_element_type=jnp.float32
    ).astype(jnp.bfloat16)
    act_grad = jnp.einsum(
        "rjd,jfd->rjf", grads_here, expert_out, preferred_element_type=jnp.float32
    )
    slots_again, act_grad = lax.optimization_barrier((slots_here, act_grad))
    hidden = jnp.einsum("rjd,jdf->rjf", slots_again, expert_in, preferred_element_type=jnp.float32)
    hidden_grad = jax.vjp(jax.nn.gelu, hidden)[1](act_grad)[0].astype(jnp.bfloat16)
    input_grad_here = jnp.einsum(
        "rjf,jdf->rjd", hidden_grad, expert_in, preferred_element_type=jnp.float32
    ).astype(jnp.bfloat16)
    returned = lax.all_to_all(
        jnp.stack([outputs_here, input_grad_here]), "expert", split_axis=1, concat_axis=2, tiled=True
    )
    outputs, inputs_grad = returned[0], returned[1]
    first_term = jnp.einsum(
        "rjd,rjf->jdf", slots_here, hidden_grad, preferred_element_type=jnp.float32
    )
    second_term = jnp.einsum(
        "rjf,rjd->jfd", activated_low, grads_here, preferred_element_type=jnp.float32
    )
    grad_in = lax.psum_scatter(
        first_term.astype(jnp.bfloat16), "dp", scatter_dimension=2, tiled=True
    ).astype(jnp.float32)
    grad_out = lax.psum_scatter(
        second_term.astype(jnp.bfloat16), "dp", scatter_dimension=1, tiled=True
    ).astype(jnp.float32)
    combine_grad = jnp.einsum("bpd,bsd->bsp", out_grad, outputs, preferred_element_type=jnp.float32)
    dispatch_grad = jnp.einsum(
        "bpd,bsd->bsp", tokens, inputs_grad, preferred_element_type=jnp.float32
    )
    logit_grad = dispatch * (
        dispatch_grad - _reduced(jnp.sum(dispatch * dispatch_grad, axis=2, keepdims=True))
    )
    logit_grad = logit_grad + combine * (
        combine_grad - _reduced(jnp.sum(combine * combine_grad, axis=1, keepdims=True))
    )
    logit_low = logit_grad.astype(jnp.bfloat16)
    first_part = jnp.einsum(
        "bsp,bsd->bpd", dispatch_low, inputs_grad, preferred_element_type=jnp.float32
    )
    second_part = jnp.einsum("bsp,ds->bpd", logit_low, router, preferred_element_type=jnp.float32)
    grad_tokens = (first_part + second_part).astype(jnp.bfloat16)
    router_term = jnp.einsum("bsp,bpd->sd", logit_low, tokens, preferred_element_type=jnp.float32)
    grad_router = _sum_everywhere(router_term, ("expert", "dp")).T
    return (grad_tokens, grad_in, grad_out, grad_router)


def solution(mesh):
    placed = (
        P(("expert", "dp"), None, None),
        P(),
        P("expert", None, None),
        P("expert", None, None),
        P(("expert", "dp"), None, None),
    )
    return jax.shard_map(
        on_device,
        mesh=mesh,
        in_specs=placed,
        out_specs=(
            P(("expert", "dp"), None, None),
            P("expert", None, "dp"),
            P("expert", "dp", None),
            P(),
        ),
        check_vma=False,
    )
```

```python
import jax
import jax.numpy as jnp
from jax import lax
from jax.sharding import PartitionSpec as P


def _tree(got):
    while len(got) > 1:
        got = [got[2 * j] + got[2 * j + 1] for j in range(len(got) // 2)]
    return got[0]


def _sum_everywhere(term, axes):
    count = 1
    for name in axes:
        count *= lax.axis_size(name)
    bits = count.bit_length() - 1
    assert 1 << bits == count and bits % 2 == 0
    pairs = lambda m: [(i, i ^ m) for i in range(count)]
    low = lax.axis_index(axes) // 4 % 4
    pieces = term.reshape(4, term.size // 4)
    got = [lax.dynamic_index_in_dim(pieces, low, 0, keepdims=False)]
    for m in range(1, 4):
        part = lax.dynamic_index_in_dim(pieces, low ^ m, 0, keepdims=False)
        got.append(lax.ppermute(part, axes, pairs(m << 2)))
    mine = _tree(got)
    for shift in [0] + list(range(4, bits, 2)):
        mine = _tree([mine] + [lax.ppermute(mine, axes, pairs(m << shift)) for m in range(1, 4)])
    got = [mine] + [lax.ppermute(mine, axes, pairs(m << 2)) for m in range(1, 4)]
    return jnp.stack([lax.select_n(low ^ q, *got) for q in range(4)]).reshape(term.shape)


def _reduced(value):
    return lax.optimization_barrier(value)


def _softmax(logits, axis):
    top = _reduced(jnp.max(logits, axis=axis, keepdims=True))
    raised = jnp.exp(logits - top)
    return raised / _reduced(jnp.sum(raised, axis=axis, keepdims=True))


def on_device(tokens, router, expert_in, expert_out, out_grad):
    logits = jnp.einsum("bpd,ds->bsp", tokens, router, preferred_element_type=jnp.float32)
    dispatch = _softmax(logits, 2)
    combine = _softmax(logits, 1)
    dispatch_low = dispatch.astype(jnp.bfloat16)
    combine_low = combine.astype(jnp.bfloat16)
    slots = jnp.einsum(
        "bsp,bpd->bsd", dispatch_low, tokens, preferred_element_type=jnp.float32
    ).astype(jnp.bfloat16)
    slot_grads = jnp.einsum(
        "bsp,bpd->bsd", combine_low, out_grad, preferred_element_type=jnp.float32
    ).astype(jnp.bfloat16)
    sent = lax.all_to_all(
        jnp.stack([slots, slot_grads]), "expert", split_axis=2, concat_axis=1, tiled=True
    )
    slots_here, grads_here = sent[0], sent[1]
    hidden = jnp.einsum("rjd,jdf->rjf", slots_here, expert_in, preferred_element_type=jnp.float32)
    activated_low = jax.nn.gelu(hidden).astype(jnp.bfloat16)
    outputs_here = jnp.einsum(
        "rjf,jfd->rjd", activated_low, expert_out, preferred_element_type=jnp.float32
    ).astype(jnp.bfloat16)
    act_grad = jnp.einsum(
        "rjd,jfd->rjf", grads_here, expert_out, preferred_element_type=jnp.float32
    )
    slots_again, act_grad = lax.optimization_barrier((slots_here, act_grad))
    hidden = jnp.einsum("rjd,jdf->rjf", slots_again, expert_in, preferred_element_type=jnp.float32)
    hidden_grad = jax.vjp(jax.nn.gelu, hidden)[1](act_grad)[0].astype(jnp.bfloat16)
    input_grad_here = jnp.einsum(
        "rjf,jdf->rjd", hidden_grad, expert_in, preferred_element_type=jnp.float32
    ).astype(jnp.bfloat16)
    returned = lax.all_to_all(
        jnp.stack([outputs_here, input_grad_here]), "expert", split_axis=1, concat_axis=2, tiled=True
    )
    outputs, inputs_grad = returned[0], returned[1]
    first_term = jnp.einsum(
        "rjd,rjf->jdf", slots_here, hidden_grad, preferred_element_type=jnp.float32
    )
    second_term = jnp.einsum(
        "rjf,rjd->jfd", activated_low, grads_here, preferred_element_type=jnp.float32
    )
    grad_in = lax.psum_scatter(
        first_term.astype(jnp.bfloat16), "dp", scatter_dimension=2, tiled=True
    ).astype(jnp.float32)
    grad_out = lax.psum_scatter(
        second_term.astype(jnp.bfloat16), "dp", scatter_dimension=1, tiled=True
    ).astype(jnp.float32)
    combine_grad = jnp.einsum("bpd,bsd->bsp", out_grad, outputs, preferred_element_type=jnp.float32)
    dispatch_grad = jnp.einsum(
        "bpd,bsd->bsp", tokens, inputs_grad, preferred_element_type=jnp.float32
    )
    logit_grad = dispatch * (
        dispatch_grad - _reduced(jnp.sum(dispatch * dispatch_grad, axis=2, keepdims=True))
    )
    logit_grad = logit_grad + combine * (
        combine_grad - _reduced(jnp.sum(combine * combine_grad, axis=1, keepdims=True))
    )
    logit_low = logit_grad.astype(jnp.bfloat16)
    first_part = jnp.einsum(
        "bsp,bsd->bpd", dispatch_low, inputs_grad, preferred_element_type=jnp.float32
    )
    second_part = jnp.einsum("bsp,ds->bpd", logit_low, router, preferred_element_type=jnp.float32)
    grad_tokens = (first_part + second_part).astype(jnp.bfloat16)
    router_term = jnp.einsum("bsp,bpd->sd", logit_low, tokens, preferred_element_type=jnp.float32)
    grad_router = _sum_everywhere(router_term, ("expert", "dp")).T
    return (grad_tokens, grad_in, grad_out, grad_router)


def solution(mesh):
    placed = (
        P(("expert", "dp"), None, None),
        P(),
        P("expert", None, None),
        P("expert", None, None),
        P(("expert", "dp"), None, None),
    )
    return jax.shard_map(
        on_device,
        mesh=mesh,
        in_specs=placed,
        out_specs=(
            P(("expert", "dp"), None, None),
            P("expert", None, "dp"),
            P("expert", "dp", None),
            P(),
        ),
        check_vma=False,
    )
```

```python
import jax
import jax.numpy as jnp
from jax import lax
from jax.sharding import PartitionSpec as P


def _tree(got):
    while len(got) > 1:
        got = [got[2 * j] + got[2 * j + 1] for j in range(len(got) // 2)]
    return got[0]


def _sum_everywhere(term, axes):
    count = 1
    for name in axes:
        count *= lax.axis_size(name)
    bits = count.bit_length() - 1
    assert 1 << bits == count and bits % 2 == 0
    pairs = lambda m: [(i, i ^ m) for i in range(count)]
    low = lax.axis_index(axes) % 4
    pieces = term.reshape(4, term.size // 4)
    got = [lax.dynamic_index_in_dim(pieces, low, 0, keepdims=False)]
    for m in range(1, 4):
        part = lax.dynamic_index_in_dim(pieces, low ^ m, 0, keepdims=False)
        got.append(lax.ppermute(part, axes, pairs(m)))
    mine = _tree(got)
    for shift in range(2, bits, 2):
        mine = _tree([mine] + [lax.ppermute(mine, axes, pairs(m << shift)) for m in range(1, 4)])
    got = [mine] + [lax.ppermute(mine, axes, pairs(m)) for m in range(1, 4)]
    return jnp.stack([lax.select_n(low ^ q, *got) for q in range(4)]).reshape(term.shape)


def _reduced(value):
    return lax.optimization_barrier(value)


def _softmax(logits, axis):
    top = _reduced(jnp.max(logits, axis=axis, keepdims=True))
    raised = jnp.exp(logits - top)
    return raised / _reduced(jnp.sum(raised, axis=axis, keepdims=True))


def on_device(tokens, router, expert_in, expert_out, out_grad):
    logits = jnp.einsum("bpd,ds->bsp", tokens, router, preferred_element_type=jnp.float32)
    dispatch = _softmax(logits, 2)
    combine = _softmax(logits, 1)
    dispatch_low = dispatch.astype(jnp.bfloat16)
    combine_low = combine.astype(jnp.bfloat16)
    slots = jnp.einsum(
        "bsp,bpd->bsd", dispatch_low, tokens, preferred_element_type=jnp.float32
    ).astype(jnp.bfloat16)
    slot_grads = jnp.einsum(
        "bsp,bpd->bsd", combine_low, out_grad, preferred_element_type=jnp.float32
    ).astype(jnp.bfloat16)
    sent = lax.all_to_all(
        jnp.stack([slots, slot_grads]), "expert", split_axis=2, concat_axis=1, tiled=True
    )
    slots_here, grads_here = sent[0], sent[1]
    hidden = jnp.einsum("rjd,jdf->rjf", slots_here, expert_in, preferred_element_type=jnp.float32)
    activated_low = jax.nn.gelu(hidden).astype(jnp.bfloat16)
    outputs_here = jnp.einsum(
        "rjf,jfd->rjd", activated_low, expert_out, preferred_element_type=jnp.float32
    ).astype(jnp.bfloat16)
    act_grad = jnp.einsum(
        "rjd,jfd->rjf", grads_here, expert_out, preferred_element_type=jnp.float32
    )
    slots_again, act_grad = lax.optimization_barrier((slots_here, act_grad))
    hidden = jnp.einsum("rjd,jdf->rjf", slots_again, expert_in, preferred_element_type=jnp.float32)
    hidden_grad = jax.vjp(jax.nn.gelu, hidden)[1](act_grad)[0].astype(jnp.bfloat16)
    input_grad_here = jnp.einsum(
        "rjf,jdf->rjd", hidden_grad, expert_in, preferred_element_type=jnp.float32
    ).astype(jnp.bfloat16)
    returned = lax.all_to_all(
        jnp.stack([outputs_here, input_grad_here]), "expert", split_axis=1, concat_axis=2, tiled=True
    )
    outputs, inputs_grad = returned[0], returned[1]
    first_term = jnp.einsum(
        "rjd,rjf->jdf", slots_here, hidden_grad, preferred_element_type=jnp.float32
    )
    slots_first, grads_first = lax.optimization_barrier((slots_here, grads_here))
    early = jnp.einsum("rjd,jdf->rjf", slots_first, expert_in, preferred_element_type=jnp.float32)
    second_term = jnp.einsum(
        "rjf,rjd->jfd", jax.nn.gelu(early).astype(jnp.bfloat16), grads_first,
        preferred_element_type=jnp.float32,
    )
    grad_in = lax.psum_scatter(
        first_term.astype(jnp.bfloat16), "dp", scatter_dimension=2, tiled=True
    ).astype(jnp.float32)
    grad_out = lax.psum_scatter(
        second_term.astype(jnp.bfloat16), "dp", scatter_dimension=1, tiled=True
    ).astype(jnp.float32)
    combine_grad = jnp.einsum("bpd,bsd->bsp", out_grad, outputs, preferred_element_type=jnp.float32)
    dispatch_grad = jnp.einsum(
        "bpd,bsd->bsp", tokens, inputs_grad, preferred_element_type=jnp.float32
    )
    logit_grad = dispatch * (
        dispatch_grad - _reduced(jnp.sum(dispatch * dispatch_grad, axis=2, keepdims=True))
    )
    logit_grad = logit_grad + combine * (
        combine_grad - _reduced(jnp.sum(combine * combine_grad, axis=1, keepdims=True))
    )
    logit_low = logit_grad.astype(jnp.bfloat16)
    first_part = jnp.einsum(
        "bsp,bsd->bpd", dispatch_low, inputs_grad, preferred_element_type=jnp.float32
    )
    second_part = jnp.einsum("bsp,ds->bpd", logit_low, router, preferred_element_type=jnp.float32)
    grad_tokens = (first_part + second_part).astype(jnp.bfloat16)
    router_term = jnp.einsum("bsp,bpd->sd", logit_low, tokens, preferred_element_type=jnp.float32)
    grad_router = _sum_everywhere(router_term, ("expert", "dp")).T
    return (grad_tokens, grad_in, grad_out, grad_router)


def solution(mesh):
    placed = (
        P(("expert", "dp"), None, None),
        P(),
        P("expert", None, None),
        P("expert", None, None),
        P(("expert", "dp"), None, None),
    )
    return jax.shard_map(
        on_device,
        mesh=mesh,
        in_specs=placed,
        out_specs=(
            P(("expert", "dp"), None, None),
            P("expert", None, "dp"),
            P("expert", "dp", None),
            P(),
        ),
        check_vma=False,
    )
```
